512 devices in a mesh: param: 32 (over x, z), ex: 16 (over y, core).
Axes of the slice: x: 4, y: 8, z: 8, core: 2. Of those that a mesh axis runs over, the one named last changes fastest.
Arguments:
- adapter_gradients: bfloat16 [512, 131072], P('ex', 'param'), may hold values from -560 to 560
- sign_hash_keys: int32 [4], replicated, may hold values from 1 to 16777215
- target_indices: int32 [256], replicated, may hold values from 0 to 511
Outputs:
- features: float32 [512, 8192], P('ex', 'param')
- scores: float32 [512, 256], P('ex')
The draws below stay inside these ranges and needn't reach their ends.
All inputs are finite; a program needn't handle non-finite values.
Results may differ from the reference program's by a relative error of at most 0.0003.
Values sent between devices are 32-bit elements; how exact they have to be, the bound alone decides.
No kernel may reach another device: no remote copies, remote signals or barrier semaphores. Data moves between devices by JAX's collectives and lax.ppermute only.
A program may use at most 128 MiB of HBM per device.

```python
import math
import jax
import jax.numpy as jnp
from jax import lax

P_SIZE = 131072
K = 8192
EX = 512
TARGETS = 256


def draw_adapter_gradients(key, part):
    noise_key, common_key, mix_key, row_key = jax.random.split(key, 4)
    position = jnp.arange(P_SIZE, dtype=jnp.float32)[None, :] / P_SIZE
    private = jax.random.truncated_normal(noise_key, -4.0, 4.0, (EX, P_SIZE), jnp.float32)
    shared = jax.random.truncated_normal(common_key, -4.0, 4.0, (1, P_SIZE), jnp.float32)
    loading = jax.random.uniform(mix_key, (EX, 1), jnp.float32, -1.5, 1.5)
    row_scale = jnp.exp(jax.random.uniform(row_key, (EX, 1), jnp.float32) * math.log(10.0))
    col_scale = jnp.exp(position * math.log(3.0))
    return (0.5 * row_scale * col_scale * (private + loading * shared)).astype(jnp.bfloat16)


def touch_ends(drawn, key, smallest, largest):
    dims = drawn.shape
    spot = [jax.random.randint(jax.random.fold_in(key, axis), (), 0, dims[axis]) for axis in range(len(dims))]
    drawn = drawn.at[tuple(spot)].set(smallest)
    longest = dims.index(max(dims))
    spot[longest] = (spot[longest] + 1) % dims[longest]
    return drawn.at[tuple(spot)].set(largest)


def setup_inputs(seed: int = 0) -> dict:
    arg_keys = jax.random.split(jax.random.key(seed), 4)
    return {
        "adapter_gradients": draw_adapter_gradients(jax.random.fold_in(arg_keys[3], 71), 0),
        "sign_hash_keys": touch_ends(jax.random.randint(arg_keys[1], (4,), 1, 16777216), jax.random.fold_in(arg_keys[1], 1), 1, 16777215).astype(jnp.int32),
        "target_indices": touch_ends(jax.random.randint(arg_keys[2], (TARGETS,), 0, EX), jax.random.fold_in(arg_keys[2], 1), 0, EX - 1).astype(jnp.int32),
    }


def sign_block(sign_hash_keys, first_row, row_count, col_count):
    mult_row = sign_hash_keys[0] | 1
    mult_col = sign_hash_keys[1] | 1
    seed_add = sign_hash_keys[2]
    mix_mult = sign_hash_keys[3] | 1
    row_ids = first_row + lax.iota(jnp.int32, row_count)[:, None]
    col_ids = lax.iota(jnp.int32, col_count)[None, :]
    hashed = row_ids * mult_row + col_ids * mult_col + seed_add
    hashed = hashed ^ lax.shift_right_logical(hashed, jnp.full_like(hashed, 16))
    hashed = hashed * mix_mult
    hashed = hashed ^ lax.shift_right_logical(hashed, jnp.full_like(hashed, 13))
    hashed = hashed * jnp.int32(-1028477387)
    hashed = hashed ^ lax.shift_right_logical(hashed, jnp.full_like(hashed, 16))
    return jnp.where(hashed < 0, 1.0, -1.0).astype(jnp.bfloat16)

def reference(adapter_gradients, sign_hash_keys, target_indices):
    rows_per_block = min(4096, P_SIZE)
    block_count = P_SIZE // rows_per_block

    def accumulate(block_idx, totals):
        first_row = block_idx * jnp.int32(rows_per_block)
        gradient_slab = lax.dynamic_slice_in_dim(adapter_gradients, first_row, rows_per_block, 1)
        signs = sign_block(sign_hash_keys, first_row, rows_per_block, K)
        return totals + jnp.dot(gradient_slab, signs, preferred_element_type=jnp.float32)
    projected = lax.fori_loop(jnp.int32(0), jnp.int32(block_count), accumulate, jnp.zeros((EX, K), jnp.float32))
    squares = lax.optimization_barrier(jnp.sum(projected * projected, axis=1, keepdims=True))
    features = projected * jnp.sqrt(jnp.float32(K) / (squares + 1e-06))
    targets = jnp.take(features, target_indices, axis=0)
    scores = jnp.dot(features, targets.T, precision=lax.Precision.HIGHEST) / jnp.float32(K)
    return (features, scores)
```

```python
import jax
import jax.numpy as jnp
from jax import lax
from jax.sharding import PartitionSpec as P

K = 8192


norm_eps = 1e-06


def sign_block(sign_hash_keys, first_row, row_count, col_count):
    mult_row = sign_hash_keys[0] | 1
    mult_col = sign_hash_keys[1] | 1
    seed_add = sign_hash_keys[2]
    mix_mult = sign_hash_keys[3] | 1
    row_ids = first_row + lax.iota(jnp.int32, row_count)[:, None]
    col_ids = lax.iota(jnp.int32, col_count)[None, :]
    hashed = row_ids * mult_row + col_ids * mult_col + seed_add
    hashed = hashed ^ lax.shift_right_logical(hashed, jnp.full_like(hashed, 16))
    hashed = hashed * mix_mult
    hashed = hashed ^ lax.shift_right_logical(hashed, jnp.full_like(hashed, 13))
    hashed = hashed * jnp.int32(-1028477387)
    hashed = hashed ^ lax.shift_right_logical(hashed, jnp.full_like(hashed, 16))
    return jnp.where(hashed < 0, 1.0, -1.0).astype(jnp.bfloat16)


def butterfly_sum(values, axis, count):
    distance = 1
    while distance < count:
        pairs = [(j, j ^ distance) for j in range(count)]
        values = values + lax.ppermute(values, axis, pairs)
        distance *= 2
    return values


def local(adapter_gradients, sign_hash_keys, target_indices):
    resident_example, resident_rows = adapter_gradients.shape
    row_base = lax.axis_index("param") * jnp.int32(resident_rows)
    turn_count = 8
    rows_per_tile = resident_rows // turn_count
    scale_k = jnp.float32(K)

    def accumulate(tile_idx, totals):
        start_offset = tile_idx * jnp.int32(rows_per_tile)
        gradient_slab = lax.dynamic_slice_in_dim(adapter_gradients, start_offset, rows_per_tile, 1)
        signs = sign_block(sign_hash_keys, row_base + start_offset, rows_per_tile, K)
        return totals + jnp.dot(gradient_slab, signs, preferred_element_type=jnp.float32)

    partial_sums = lax.fori_loop(
        jnp.int32(0),
        jnp.int32(turn_count),
        accumulate,
        jnp.zeros((resident_example, K), jnp.float32),
    )
    param_count = lax.psum(1, "param")
    col_width = K // param_count
    blocks = partial_sums.reshape(resident_example, param_count, col_width)
    blocks = lax.all_to_all(blocks, "param", 1, 1, tiled=True)
    projected = jnp.sum(blocks, axis=1)
    pool_rows = lax.all_gather(projected, "ex", axis=0, tiled=True)
    target_rows = jnp.take(pool_rows, target_indices, axis=0)
    partial_dots = jnp.dot(projected, target_rows.T, precision=lax.Precision.HIGHEST)
    own_squares = jnp.sum(projected * projected, axis=1)
    target_squares = jnp.sum(target_rows * target_rows, axis=1)
    packed = jnp.concatenate([partial_dots.reshape(-1), own_squares, target_squares])
    packed = butterfly_sum(packed, "param", param_count)
    dot_count = partial_dots.size
    dots = packed[:dot_count].reshape(partial_dots.shape)
    total_sq = packed[dot_count:dot_count + resident_example]
    target_sq = packed[dot_count + resident_example:]
    own_scale = jnp.sqrt(scale_k / (total_sq + norm_eps))
    target_scale = jnp.sqrt(scale_k / (target_sq + norm_eps))
    features = projected * own_scale[:, None]
    scores = dots * own_scale[:, None] * target_scale[None, :] / scale_k
    return (features, scores)


def solution(mesh):
    return jax.shard_map(
        local,
        mesh=mesh,
        in_specs=(P("ex", "param"), P(), P()),
        out_specs=(P("ex", "param"), P("ex", None)),
        check_vma=False,
    )
```

```python
import jax
import jax.numpy as jnp
from jax import lax
from jax.sharding import PartitionSpec as P

K = 8192


norm_eps = 1e-06


def sign_block(sign_hash_keys, first_row, row_count, col_ids):
    mult_row = sign_hash_keys[0] | 1
    mult_col = sign_hash_keys[1] | 1
    seed_add = sign_hash_keys[2]
    mix_mult = sign_hash_keys[3] | 1
    row_ids = first_row + lax.iota(jnp.int32, row_count)[:, None]
    hashed = row_ids * mult_row + col_ids[None, :] * mult_col + seed_add
    hashed = hashed ^ lax.shift_right_logical(hashed, jnp.full_like(hashed, 16))
    hashed = hashed * mix_mult
    hashed = hashed ^ lax.shift_right_logical(hashed, jnp.full_like(hashed, 13))
    hashed = hashed * jnp.int32(-1028477387)
    hashed = hashed ^ lax.shift_right_logical(hashed, jnp.full_like(hashed, 16))
    return jnp.where(hashed < 0, 1.0, -1.0).astype(jnp.bfloat16)


def butterfly_sum(values, axis, count):
    distance = 1
    while distance < count:
        pairs = [(j, j ^ distance) for j in range(count)]
        values = values + lax.ppermute(values, axis, pairs)
        distance *= 2
    return values


def local(adapter_gradients, sign_hash_keys, target_indices):
    resident_example, resident_rows = adapter_gradients.shape
    row_base = lax.axis_index("param") * jnp.int32(resident_rows)
    turn_count = 8
    rows_per_tile = resident_rows // turn_count
    scale_k = jnp.float32(K)
    param_count = lax.psum(1, "param")
    col_width = K // param_count
    chunk_count = 2
    chunk_width = col_width // chunk_count

    pieces = []
    for chunk in range(chunk_count):
        owner = lax.iota(jnp.int32, param_count)[:, None] * col_width
        col_ids = (owner + chunk * chunk_width + lax.iota(jnp.int32, chunk_width)[None, :]).reshape(-1)
        totals = None
        for tile in range(turn_count):
            start_offset = tile * rows_per_tile
            gradient_slab = adapter_gradients[:, start_offset:start_offset + rows_per_tile]
            signs = sign_block(sign_hash_keys, row_base + start_offset, rows_per_tile, col_ids)
            term = jnp.dot(gradient_slab, signs, preferred_element_type=jnp.float32)
            totals = term if totals is None else totals + term
        blocks = totals.reshape(resident_example, param_count, chunk_width)
        blocks = lax.all_to_all(blocks, "param", 1, 1, tiled=True)
        pieces.append(jnp.sum(blocks, axis=1))
    projected = jnp.concatenate(pieces, axis=1)
    pool_rows = lax.all_gather(projected, "ex", axis=0, tiled=True)
    target_rows = jnp.take(pool_rows, target_indices, axis=0)
    partial_dots = jnp.dot(projected, target_rows.T, precision=lax.Precision.HIGHEST)
    own_squares = jnp.sum(projected * projected, axis=1)
    target_squares = jnp.sum(target_rows * target_rows, axis=1)
    packed = jnp.concatenate([partial_dots.reshape(-1), own_squares, target_squares])
    packed = butterfly_sum(packed, "param", param_count)
    dot_count = partial_dots.size
    dots = packed[:dot_count].reshape(partial_dots.shape)
    total_sq = packed[dot_count:dot_count + resident_example]
    target_sq = packed[dot_count + resident_example:]
    own_scale = jnp.sqrt(scale_k / (total_sq + norm_eps))
    target_scale = jnp.sqrt(scale_k / (target_sq + norm_eps))
    features = projected * own_scale[:, None]
    scores = dots * own_scale[:, None] * target_scale[None, :] / scale_k
    return (features, scores)


def solution(mesh):
    return jax.shard_map(
        local,
        mesh=mesh,
        in_specs=(P("ex", "param"), P(), P()),
        out_specs=(P("ex", "param"), P("ex", None)),
        check_vma=False,
    )
```

```python
import jax
import jax.numpy as jnp
from jax import lax
from jax.sharding import Mesh, PartitionSpec as P

K = 8192


norm_eps = 1e-06


def sign_block(sign_hash_keys, first_row, row_count, col_ids):
    mult_row = sign_hash_keys[0] | 1
    mult_col = sign_hash_keys[1] | 1
    seed_add = sign_hash_keys[2]
    mix_mult = sign_hash_keys[3] | 1
    row_ids = first_row + lax.iota(jnp.int32, row_count)[:, None]
    hashed = row_ids * mult_row + col_ids[None, :] * mult_col + seed_add
    hashed = hashed ^ lax.shift_right_logical(hashed, jnp.full_like(hashed, 16))
    hashed = hashed * mix_mult
    hashed = hashed ^ lax.shift_right_logical(hashed, jnp.full_like(hashed, 13))
    hashed = hashed * jnp.int32(-1028477387)
    hashed = hashed ^ lax.shift_right_logical(hashed, jnp.full_like(hashed, 16))
    return jnp.where(hashed < 0, 1.0, -1.0).astype(jnp.bfloat16)


def butterfly_sum(values, axis, count):
    distance = 1
    while distance < count:
        pairs = [(j, j ^ distance) for j in range(count)]
        values = values + lax.ppermute(values, axis, pairs)
        distance *= 2
    return values


def local(adapter_gradients, sign_hash_keys, target_indices):
    resident_example, resident_rows = adapter_gradients.shape
    row_base = lax.axis_index("param") * jnp.int32(resident_rows)
    core = lax.axis_index("ec")
    swap = [(0, 1), (1, 0)]
    turn_count = 8
    rows_per_tile = resident_rows // turn_count
    scale_k = jnp.float32(K)
    param_count = lax.psum(1, "param")
    col_width = K // param_count
    half_width = col_width // 2

    unit = ((sign_hash_keys[3] | 1) & 1).astype(jnp.float32)
    partner = lax.ppermute(adapter_gradients.astype(jnp.float32), "ec", swap) * unit
    pair_gradients = jnp.concatenate([adapter_gradients, partner.astype(jnp.bfloat16)], axis=0)
    owner = lax.iota(jnp.int32, param_count)[:, None] * col_width
    col_ids = (owner + core * half_width + lax.iota(jnp.int32, half_width)[None, :]).reshape(-1)
    totals = None
    for tile in range(turn_count):
        start_offset = tile * rows_per_tile
        gradient_slab = pair_gradients[:, start_offset:start_offset + rows_per_tile]
        signs = sign_block(sign_hash_keys, row_base + start_offset, rows_per_tile, col_ids)
        term = jnp.dot(gradient_slab, signs, preferred_element_type=jnp.float32)
        totals = term if totals is None else totals + term

    pair_rows = 2 * resident_example
    blocks = totals.reshape(pair_rows, param_count, half_width)
    blocks = lax.all_to_all(blocks, "param", 1, 1, tiled=True)
    pair_projected = jnp.sum(blocks, axis=1)
    mine = pair_projected[:resident_example]
    theirs = lax.ppermute(pair_projected[resident_example:], "ec", swap)
    projected = jnp.where(core == 0, jnp.concatenate([mine, theirs], axis=1), jnp.concatenate([theirs, mine], axis=1))

    pool_rows = lax.all_gather(pair_projected, "ey", axis=0, tiled=True)
    wanted_core = (target_indices // resident_example) % 2
    positions = (target_indices // pair_rows) * pair_rows + (wanted_core ^ core) * resident_example + target_indices % resident_example
    target_rows = jnp.take(pool_rows, positions, axis=0)
    partial_dots = jnp.dot(pair_projected, target_rows.T, precision=lax.Precision.HIGHEST)
    pair_squares = jnp.sum(pair_projected * pair_projected, axis=1)
    target_squares = jnp.sum(target_rows * target_rows, axis=1)
    outgoing = jnp.concatenate([partial_dots[resident_example:].reshape(-1), pair_squares[resident_example:], target_squares])
    kept = jnp.concatenate([partial_dots[:resident_example].reshape(-1), pair_squares[:resident_example], target_squares])
    packed = kept + lax.ppermute(outgoing, "ec", swap)
    packed = butterfly_sum(packed, "param", param_count)
    dot_count = resident_example * target_rows.shape[0]
    dots = packed[:dot_count].reshape(resident_example, target_rows.shape[0])
    total_sq = packed[dot_count:dot_count + resident_example]
    target_sq = packed[dot_count + resident_example:]
    own_scale = jnp.sqrt(scale_k / (total_sq + norm_eps))
    target_scale = jnp.sqrt(scale_k / (target_sq + norm_eps))
    features = projected * own_scale[:, None]
    scores = dots * own_scale[:, None] * target_scale[None, :] / scale_k
    return (features, scores)


def solution(mesh):
    devices = mesh.devices
    pair_mesh = Mesh(devices.reshape(devices.shape[0], devices.shape[1] // 2, 2), ("param", "ey", "ec"))
    return jax.shard_map(
        local,
        mesh=pair_mesh,
        in_specs=(P(("ey", "ec"), "param"), P(), P()),
        out_specs=(P(("ey", "ec"), "param"), P(("ey", "ec"), None)),
        check_vma=False,
    )
```

```python
import jax
import jax.numpy as jnp
from jax import lax
from jax.sharding import Mesh, PartitionSpec as P

K = 8192


norm_eps = 1e-06


def sign_block(sign_hash_keys, first_row, row_count, col_ids):
    mult_row = sign_hash_keys[0] | 1
    mult_col = sign_hash_keys[1] | 1
    seed_add = sign_hash_keys[2]
    mix_mult = sign_hash_keys[3] | 1
    row_ids = first_row + lax.iota(jnp.int32, row_count)[:, None]
    hashed = row_ids * mult_row + col_ids[None, :] * mult_col + seed_add
    hashed = hashed ^ lax.shift_right_logical(hashed, jnp.full_like(hashed, 16))
    hashed = hashed * mix_mult
    hashed = hashed ^ lax.shift_right_logical(hashed, jnp.full_like(hashed, 13))
    hashed = hashed * jnp.int32(-1028477387)
    hashed = hashed ^ lax.shift_right_logical(hashed, jnp.full_like(hashed, 16))
    return jnp.where(hashed < 0, 1.0, -1.0).astype(jnp.bfloat16)


def butterfly_sum(values, axis, count):
    distance = 1
    while distance < count:
        pairs = [(j, j ^ distance) for j in range(count)]
        values = values + lax.ppermute(values, axis, pairs)
        distance *= 2
    return values


def local(adapter_gradients, sign_hash_keys, target_indices):
    resident_example, resident_rows = adapter_gradients.shape
    row_base = lax.axis_index("param") * jnp.int32(resident_rows)
    core = lax.axis_index("ec")
    swap = [(0, 1), (1, 0)]
    turn_count = 8
    rows_per_tile = resident_rows // turn_count
    scale_k = jnp.float32(K)
    param_count = lax.psum(1, "param")
    col_width = K // param_count
    half_width = col_width // 2

    unit = ((sign_hash_keys[3] | 1) & 1).astype(jnp.float32)
    partner = lax.ppermute(adapter_gradients.astype(jnp.float32), "ec", swap) * unit
    partner = partner.astype(jnp.bfloat16)
    pair_gradients = jnp.where(
        core == 0,
        jnp.concatenate([adapter_gradients, partner], axis=0),
        jnp.concatenate([partner, adapter_gradients], axis=0),
    )
    owner = lax.iota(jnp.int32, param_count)[:, None] * col_width
    col_ids = (owner + core * half_width + lax.iota(jnp.int32, half_width)[None, :]).reshape(-1)
    totals = None
    for tile in range(turn_count):
        start_offset = tile * rows_per_tile
        gradient_slab = pair_gradients[:, start_offset:start_offset + rows_per_tile]
        signs = sign_block(sign_hash_keys, row_base + start_offset, rows_per_tile, col_ids)
        term = jnp.dot(gradient_slab, signs, preferred_element_type=jnp.float32)
        totals = term if totals is None else totals + term

    blocks = totals.reshape(2, resident_example, param_count, half_width)
    blocks = jnp.transpose(blocks, (2, 0, 1, 3)).reshape(2 * param_count, resident_example, half_width)
    blocks = lax.all_to_all(blocks, ("param", "ec"), 0, 0, tiled=True)
    blocks = jnp.sum(blocks.reshape(param_count, 2, resident_example, half_width), axis=0)
    projected = jnp.transpose(blocks, (1, 0, 2)).reshape(resident_example, col_width)

    pool_rows = lax.all_gather(projected, ("ey", "ec"), axis=0, tiled=True)
    target_rows = jnp.take(pool_rows, target_indices, axis=0)
    partial_dots = jnp.dot(projected, target_rows.T, precision=lax.Precision.HIGHEST)
    own_squares = jnp.sum(projected * projected, axis=1)
    target_squares = jnp.sum(target_rows * target_rows, axis=1)
    packed = jnp.concatenate([partial_dots.reshape(-1), own_squares, target_squares])
    packed = butterfly_sum(packed, "param", param_count)
    dot_count = partial_dots.size
    dots = packed[:dot_count].reshape(partial_dots.shape)
    total_sq = packed[dot_count:dot_count + resident_example]
    target_sq = packed[dot_count + resident_example:]
    own_scale = jnp.sqrt(scale_k / (total_sq + norm_eps))
    target_scale = jnp.sqrt(scale_k / (target_sq + norm_eps))
    features = projected * own_scale[:, None]
    scores = dots * own_scale[:, None] * target_scale[None, :] / scale_k
    return (features, scores)


def solution(mesh):
    devices = mesh.devices
    pair_mesh = Mesh(devices.reshape(devices.shape[0], devices.shape[1] // 2, 2), ("param", "ey", "ec"))
    return jax.shard_map(
        local,
        mesh=pair_mesh,
        in_specs=(P(("ey", "ec"), "param"), P(), P()),
        out_specs=(P(("ey", "ec"), "param"), P(("ey", "ec"), None)),
        check_vma=False,
    )
```

```python
import jax
import jax.numpy as jnp
from jax import lax
from jax.sharding import Mesh, PartitionSpec as P

K = 8192


norm_eps = 1e-06


def sign_block(sign_hash_keys, first_row, row_count, col_ids):
    mult_row = sign_hash_keys[0] | 1
    mult_col = sign_hash_keys[1] | 1
    seed_add = sign_hash_keys[2]
    mix_mult = sign_hash_keys[3] | 1
    row_ids = first_row + lax.iota(jnp.int32, row_count)[:, None]
    hashed = row_ids * mult_row + col_ids[None, :] * mult_col + seed_add
    hashed = hashed ^ lax.shift_right_logical(hashed, jnp.full_like(hashed, 16))
    hashed = hashed * mix_mult
    hashed = hashed ^ lax.shift_right_logical(hashed, jnp.full_like(hashed, 13))
    hashed = hashed * jnp.int32(-1028477387)
    hashed = hashed ^ lax.shift_right_logical(hashed, jnp.full_like(hashed, 16))
    return jnp.where(hashed < 0, 1.0, -1.0).astype(jnp.bfloat16)


def butterfly_sum(values, axis, count):
    distance = 1
    while distance < count:
        pairs = [(j, j ^ distance) for j in range(count)]
        values = values + lax.ppermute(values, axis, pairs)
        distance *= 2
    return values


def local(adapter_gradients, sign_hash_keys, target_indices):
    resident_example, resident_rows = adapter_gradients.shape
    row_base = lax.axis_index("param") * jnp.int32(resident_rows)
    core = lax.axis_index("ec")
    swap = [(0, 1), (1, 0)]
    scale_k = jnp.float32(K)
    param_count = lax.psum(1, "param")
    col_width = K // param_count
    half_width = col_width // 2

    unit = ((sign_hash_keys[3] | 1) & 1).astype(jnp.float32)
    partner = lax.ppermute(adapter_gradients.astype(jnp.float32), "ec", swap) * unit
    partner = partner.astype(jnp.bfloat16)
    pair_gradients = jnp.where(
        core == 0,
        jnp.concatenate([adapter_gradients, partner], axis=0),
        jnp.concatenate([partner, adapter_gradients], axis=0),
    )
    chunk_count = 2
    chunk_width = half_width // chunk_count
    tile_count = 4
    rows_per_tile = resident_rows // tile_count
    owner = lax.iota(jnp.int32, param_count)[:, None] * col_width
    pieces = []
    for chunk in range(chunk_count):
        first_col = core * half_width + chunk * chunk_width
        col_ids = (owner + first_col + lax.iota(jnp.int32, chunk_width)[None, :]).reshape(-1)
        totals = None
        for tile in range(tile_count):
            start_offset = tile * rows_per_tile
            gradient_slab = pair_gradients[:, start_offset:start_offset + rows_per_tile]
            signs = sign_block(sign_hash_keys, row_base + start_offset, rows_per_tile, col_ids)
            term = jnp.dot(gradient_slab, signs, preferred_element_type=jnp.float32)
            totals = term if totals is None else totals + term
        blocks = totals.reshape(2, resident_example, param_count, chunk_width)
        blocks = jnp.transpose(blocks, (2, 0, 1, 3)).reshape(2 * param_count, resident_example, chunk_width)
        blocks = lax.all_to_all(blocks, ("param", "ec"), 0, 0, tiled=True)
        pieces.append(jnp.sum(blocks.reshape(param_count, 2, resident_example, chunk_width), axis=0))
    projected = jnp.transpose(jnp.stack(pieces), (2, 1, 0, 3)).reshape(resident_example, col_width)

    pool_rows = lax.all_gather(projected, ("ey", "ec"), axis=0, tiled=True)
    target_rows = jnp.take(pool_rows, target_indices, axis=0)
    partial_dots = jnp.dot(projected, target_rows.T, precision=lax.Precision.HIGHEST)
    own_squares = jnp.sum(projected * projected, axis=1)
    target_squares = jnp.sum(target_rows * target_rows, axis=1)
    packed = jnp.concatenate([partial_dots.reshape(-1), own_squares, target_squares])
    packed = butterfly_sum(packed, "param", param_count)
    dot_count = partial_dots.size
    dots = packed[:dot_count].reshape(partial_dots.shape)
    total_sq = packed[dot_count:dot_count + resident_example]
    target_sq = packed[dot_count + resident_example:]
    own_scale = jnp.sqrt(scale_k / (total_sq + norm_eps))
    target_scale = jnp.sqrt(scale_k / (target_sq + norm_eps))
    features = projected * own_scale[:, None]
    scores = dots * own_scale[:, None] * target_scale[None, :] / scale_k
    return (features, scores)


def solution(mesh):
    devices = mesh.devices
    pair_mesh = Mesh(devices.reshape(devices.shape[0], devices.shape[1] // 2, 2), ("param", "ey", "ec"))
    return jax.shard_map(
        local,
        mesh=pair_mesh,
        in_specs=(P(("ey", "ec"), "param"), P(), P()),
        out_specs=(P(("ey", "ec"), "param"), P(("ey", "ec"), None)),
        check_vma=False,
    )
```

```python
import jax
import jax.numpy as jnp
from jax import lax
from jax.sharding import Mesh, PartitionSpec as P

K = 8192


norm_eps = 1e-06


def sign_block(sign_hash_keys, first_row, row_count, col_ids):
    mult_row = sign_hash_keys[0] | 1
    mult_col = sign_hash_keys[1] | 1
    seed_add = sign_hash_keys[2]
    mix_mult = sign_hash_keys[3] | 1
    row_ids = first_row + lax.iota(jnp.int32, row_count)
    row_terms = row_ids * mult_row + seed_add
    col_terms = col_ids * mult_col
    hashed = row_terms[:, None] + col_terms[None, :]
    hashed = hashed ^ lax.shift_right_logical(hashed, jnp.full_like(hashed, 16))
    hashed = hashed * mix_mult
    hashed = hashed ^ lax.shift_right_logical(hashed, jnp.full_like(hashed, 13))
    hashed = hashed * jnp.int32(-1028477387)
    hashed = hashed ^ lax.shift_right_logical(hashed, jnp.full_like(hashed, 16))
    return jnp.where(hashed < 0, jnp.bfloat16(1.0), jnp.bfloat16(-1.0))


def butterfly_sum(values, axis, count):
    distance = 1
    while distance < count:
        pairs = [(j, j ^ distance) for j in range(count)]
        values = values + lax.ppermute(values, axis, pairs)
        distance *= 2
    return values


def local(adapter_gradients, sign_hash_keys, target_indices):
    resident_example, resident_rows = adapter_gradients.shape
    row_base = lax.axis_index("param") * jnp.int32(resident_rows)
    core = lax.axis_index("ec")
    swap = [(0, 1), (1, 0)]
    turn_count = 8
    rows_per_tile = resident_rows // turn_count
    scale_k = jnp.float32(K)
    param_count = lax.psum(1, "param")
    col_width = K // param_count
    half_width = col_width // 2

    unit = ((sign_hash_keys[3] | 1) & 1).astype(jnp.float32)
    partner = lax.ppermute(adapter_gradients.astype(jnp.float32), "ec", swap) * unit
    partner = partner.astype(jnp.bfloat16)
    pair_gradients = jnp.where(
        core == 0,
        jnp.concatenate([adapter_gradients, partner], axis=0),
        jnp.concatenate([partner, adapter_gradients], axis=0),
    )
    owner = lax.iota(jnp.int32, param_count)[:, None] * col_width
    col_ids = (owner + core * half_width + lax.iota(jnp.int32, half_width)[None, :]).reshape(-1)
    totals = None
    for tile in range(turn_count):
        start_offset = tile * rows_per_tile
        gradient_slab = pair_gradients[:, start_offset:start_offset + rows_per_tile]
        signs = sign_block(sign_hash_keys, row_base + start_offset, rows_per_tile, col_ids)
        term = jnp.dot(gradient_slab, signs, preferred_element_type=jnp.float32)
        totals = term if totals is None else totals + term

    blocks = totals.reshape(2, resident_example, param_count, half_width)
    blocks = jnp.transpose(blocks, (2, 0, 1, 3)).reshape(2 * param_count, resident_example, half_width)
    blocks = lax.all_to_all(blocks, ("param", "ec"), 0, 0, tiled=True)
    blocks = jnp.sum(blocks.reshape(param_count, 2, resident_example, half_width), axis=0)
    projected = jnp.transpose(blocks, (1, 0, 2)).reshape(resident_example, col_width)

    pool_rows = lax.all_gather(projected, ("ey", "ec"), axis=0, tiled=True)
    target_rows = jnp.take(pool_rows, target_indices, axis=0)
    partial_dots = jnp.dot(projected, target_rows.T, precision=lax.Precision.HIGHEST)
    own_squares = jnp.sum(projected * projected, axis=1)
    target_squares = jnp.sum(target_rows * target_rows, axis=1)
    packed = jnp.concatenate([partial_dots.reshape(-1), own_squares, target_squares])
    packed = butterfly_sum(packed, "param", param_count)
    dot_count = partial_dots.size
    dots = packed[:dot_count].reshape(partial_dots.shape)
    total_sq = packed[dot_count:dot_count + resident_example]
    target_sq = packed[dot_count + resident_example:]
    own_scale = jnp.sqrt(scale_k / (total_sq + norm_eps))
    target_scale = jnp.sqrt(scale_k / (target_sq + norm_eps))
    features = projected * own_scale[:, None]
    scores = dots * own_scale[:, None] * target_scale[None, :] / scale_k
    return (features, scores)


def solution(mesh):
    devices = mesh.devices
    pair_mesh = Mesh(devices.reshape(devices.shape[0], devices.shape[1] // 2, 2), ("param", "ey", "ec"))
    return jax.shard_map(
        local,
        mesh=pair_mesh,
        in_specs=(P(("ey", "ec"), "param"), P(), P()),
        out_specs=(P(("ey", "ec"), "param"), P(("ey", "ec"), None)),
        check_vma=False,
    )
```

```python
import jax
import jax.numpy as jnp
from jax import lax
from jax.sharding import Mesh, PartitionSpec as P

K = 8192


norm_eps = 1e-06


def hash_terms(sign_hash_keys, first_row, row_count, col_ids):
    mult_row = sign_hash_keys[0] | 1
    mult_col = sign_hash_keys[1] | 1
    seed_add = sign_hash_keys[2]
    row_ids = first_row + lax.iota(jnp.int32, row_count)
    return row_ids * mult_row + seed_add, col_ids * mult_col


def sign_block(sign_hash_keys, row_terms, col_terms):
    mix_mult = sign_hash_keys[3] | 1
    hashed = row_terms[:, None] + col_terms[None, :]
    hashed = hashed ^ lax.shift_right_logical(hashed, jnp.full_like(hashed, 16))
    hashed = hashed * mix_mult
    hashed = hashed ^ lax.shift_right_logical(hashed, jnp.full_like(hashed, 13))
    hashed = hashed * jnp.int32(-1028477387)
    hashed = hashed ^ lax.shift_right_logical(hashed, jnp.full_like(hashed, 16))
    return jnp.where(hashed < 0, jnp.bfloat16(1.0), jnp.bfloat16(-1.0))


def butterfly_sum(values, axis, count):
    distance = 1
    while distance < count:
        pairs = [(j, j ^ distance) for j in range(count)]
        values = values + lax.ppermute(values, axis, pairs)
        distance *= 2
    return values


def local(adapter_gradients, sign_hash_keys, target_indices):
    resident_example, resident_rows = adapter_gradients.shape
    row_base = lax.axis_index("param") * jnp.int32(resident_rows)
    core = lax.axis_index("ec")
    swap = [(0, 1), (1, 0)]
    turn_count = 8
    rows_per_tile = resident_rows // turn_count
    scale_k = jnp.float32(K)
    param_count = lax.psum(1, "param")
    col_width = K // param_count
    half_width = col_width // 2

    unit = ((sign_hash_keys[3] | 1) & 1).astype(jnp.float32)
    partner = lax.ppermute(adapter_gradients.astype(jnp.float32), "ec", swap) * unit
    partner = partner.astype(jnp.bfloat16)
    pair_gradients = jnp.where(
        core == 0,
        jnp.concatenate([adapter_gradients, partner], axis=0),
        jnp.concatenate([partner, adapter_gradients], axis=0),
    )
    owner = lax.iota(jnp.int32, param_count)[:, None] * col_width
    col_ids = (owner + core * half_width + lax.iota(jnp.int32, half_width)[None, :]).reshape(-1)
    row_terms, col_terms = hash_terms(sign_hash_keys, row_base, resident_rows, col_ids)
    totals = None
    for tile in range(turn_count):
        start_offset = tile * rows_per_tile
        gradient_slab = pair_gradients[:, start_offset:start_offset + rows_per_tile]
        signs = sign_block(sign_hash_keys, row_terms[start_offset:start_offset + rows_per_tile], col_terms)
        term = jnp.dot(gradient_slab, signs, preferred_element_type=jnp.float32)
        totals = term if totals is None else totals + term

    blocks = totals.reshape(2, resident_example, param_count, half_width)
    blocks = jnp.transpose(blocks, (2, 0, 1, 3)).reshape(2 * param_count, resident_example, half_width)
    blocks = lax.all_to_all(blocks, ("param", "ec"), 0, 0, tiled=True)
    blocks = jnp.sum(blocks.reshape(param_count, 2, resident_example, half_width), axis=0)
    projected = jnp.transpose(blocks, (1, 0, 2)).reshape(resident_example, col_width)

    pool_rows = lax.all_gather(projected, ("ey", "ec"), axis=0, tiled=True)
    target_rows = jnp.take(pool_rows, target_indices, axis=0)
    partial_dots = jnp.dot(projected, target_rows.T, precision=lax.Precision.HIGHEST)
    own_squares = jnp.sum(projected * projected, axis=1)
    target_squares = jnp.sum(target_rows * target_rows, axis=1)
    packed = jnp.concatenate([partial_dots.reshape(-1), own_squares, target_squares])
    packed = butterfly_sum(packed, "param", param_count)
    dot_count = partial_dots.size
    dots = packed[:dot_count].reshape(partial_dots.shape)
    total_sq = packed[dot_count:dot_count + resident_example]
    target_sq = packed[dot_count + resident_example:]
    own_scale = jnp.sqrt(scale_k / (total_sq + norm_eps))
    target_scale = jnp.sqrt(scale_k / (target_sq + norm_eps))
    features = projected * own_scale[:, None]
    scores = dots * own_scale[:, None] * target_scale[None, :] / scale_k
    return (features, scores)


def solution(mesh):
    devices = mesh.devices
    pair_mesh = Mesh(devices.reshape(devices.shape[0], devices.shape[1] // 2, 2), ("param", "ey", "ec"))
    return jax.shard_map(
        local,
        mesh=pair_mesh,
        in_specs=(P(("ey", "ec"), "param"), P(), P()),
        out_specs=(P(("ey", "ec"), "param"), P(("ey", "ec"), None)),
        check_vma=False,
    )
```

```python
import jax
import jax.numpy as jnp
from jax import lax
from jax.sharding import Mesh, PartitionSpec as P

K = 8192


norm_eps = 1e-06


def hash_terms(sign_hash_keys, first_row, row_count, col_ids):
    mult_row = sign_hash_keys[0] | 1
    mult_col = sign_hash_keys[1] | 1
    seed_add = sign_hash_keys[2]
    row_ids = first_row + lax.iota(jnp.int32, row_count)
    return row_ids * mult_row + seed_add, col_ids * mult_col


def sign_block(sign_hash_keys, row_terms, col_terms):
    mix_mult = sign_hash_keys[3] | 1
    hashed = row_terms[:, None] + col_terms[None, :]
    hashed = hashed ^ lax.shift_right_logical(hashed, jnp.full_like(hashed, 16))
    hashed = hashed * mix_mult
    hashed = hashed ^ lax.shift_right_logical(hashed, jnp.full_like(hashed, 13))
    hashed = hashed * jnp.int32(-1028477387)
    hashed = hashed ^ lax.shift_right_logical(hashed, jnp.full_like(hashed, 16))
    return jnp.where(hashed < 0, jnp.bfloat16(1.0), jnp.bfloat16(-1.0))


def butterfly_sum(values, axis, count):
    distance = 1
    while distance < count:
        pairs = [(j, j ^ distance) for j in range(count)]
        values = values + lax.ppermute(values, axis, pairs)
        distance *= 2
    return values


def local(adapter_gradients, sign_hash_keys, target_indices):
    resident_example, resident_rows = adapter_gradients.shape
    row_base = lax.axis_index("param") * jnp.int32(resident_rows)
    core = lax.axis_index("ec")
    swap = [(0, 1), (1, 0)]
    turn_count = 8
    rows_per_tile = resident_rows // turn_count
    scale_k = jnp.float32(K)
    param_count = lax.psum(1, "param")
    col_width = K // param_count
    half_width = col_width // 2

    unit = ((sign_hash_keys[3] | 1) & 1).astype(jnp.float32)
    partner = lax.ppermute(adapter_gradients.astype(jnp.float32), "ec", swap) * unit
    partner = partner.astype(jnp.bfloat16)
    pair_gradients = jnp.where(
        core == 0,
        jnp.concatenate([adapter_gradients, partner], axis=0),
        jnp.concatenate([partner, adapter_gradients], axis=0),
    )
    owner = lax.iota(jnp.int32, param_count)[:, None] * col_width
    col_ids = (owner + core * half_width + lax.iota(jnp.int32, half_width)[None, :]).reshape(-1)
    row_terms, col_terms = hash_terms(sign_hash_keys, row_base, resident_rows, col_ids)
    totals = None
    for tile in range(turn_count):
        start_offset = tile * rows_per_tile
        gradient_slab = pair_gradients[:, start_offset:start_offset + rows_per_tile]
        signs = sign_block(sign_hash_keys, row_terms[start_offset:start_offset + rows_per_tile], col_terms)
        term = jnp.einsum(
            "cra,apj->pcrj",
            gradient_slab.reshape(2, resident_example, rows_per_tile),
            signs.reshape(rows_per_tile, param_count, half_width),
            preferred_element_type=jnp.float32,
        )
        totals = term if totals is None else totals + term

    blocks = totals.reshape(2 * param_count, resident_example, half_width)
    blocks = lax.all_to_all(blocks, ("param", "ec"), 0, 0, tiled=True)
    blocks = jnp.sum(blocks.reshape(param_count, 2, resident_example, half_width), axis=0)
    projected = jnp.transpose(blocks, (1, 0, 2)).reshape(resident_example, col_width)

    pool_rows = lax.all_gather(projected, ("ey", "ec"), axis=0, tiled=True)
    target_rows = jnp.take(pool_rows, target_indices, axis=0)
    partial_dots = jnp.dot(projected, target_rows.T, precision=lax.Precision.HIGHEST)
    own_squares = jnp.sum(projected * projected, axis=1)
    target_squares = jnp.sum(target_rows * target_rows, axis=1)
    packed = jnp.concatenate([partial_dots.reshape(-1), own_squares, target_squares])
    packed = butterfly_sum(packed, "param", param_count)
    dot_count = partial_dots.size
    dots = packed[:dot_count].reshape(partial_dots.shape)
    total_sq = packed[dot_count:dot_count + resident_example]
    target_sq = packed[dot_count + resident_example:]
    own_scale = jnp.sqrt(scale_k / (total_sq + norm_eps))
    target_scale = jnp.sqrt(scale_k / (target_sq + norm_eps))
    features = projected * own_scale[:, None]
    scores = dots * own_scale[:, None] * target_scale[None, :] / scale_k
    return (features, scores)


def solution(mesh):
    devices = mesh.devices
    pair_mesh = Mesh(devices.reshape(devices.shape[0], devices.shape[1] // 2, 2), ("param", "ey", "ec"))
    return jax.shard_map(
        local,
        mesh=pair_mesh,
        in_specs=(P(("ey", "ec"), "param"), P(), P()),
        out_specs=(P(("ey", "ec"), "param"), P(("ey", "ec"), None)),
        check_vma=False,
    )
```

```python
import jax
import jax.numpy as jnp
from jax import lax
from jax.sharding import Mesh, PartitionSpec as P

K = 8192


norm_eps = 1e-06


def hash_terms(hash_scalars, first_row, row_count, col_ids):
    mult_row, mult_col, seed_add, _ = hash_scalars
    row_ids = first_row + lax.iota(jnp.int32, row_count)
    return row_ids * mult_row + seed_add, col_ids * mult_col


def sign_block(hash_scalars, row_terms, col_terms):
    mix_mult = hash_scalars[3]
    hashed = row_terms[:, None] + col_terms[None, :]
    hashed = hashed ^ lax.shift_right_logical(hashed, jnp.full_like(hashed, 16))
    hashed = hashed * mix_mult
    hashed = hashed ^ lax.shift_right_logical(hashed, jnp.full_like(hashed, 13))
    hashed = hashed * jnp.int32(-1028477387)
    hashed = hashed ^ lax.shift_right_logical(hashed, jnp.full_like(hashed, 16))
    return jnp.where(hashed < 0, jnp.bfloat16(1.0), jnp.bfloat16(-1.0))


def butterfly_sum(values, axis, count):
    distance = 1
    while distance < count:
        pairs = [(j, j ^ distance) for j in range(count)]
        values = values + lax.ppermute(values, axis, pairs)
        distance *= 2
    return values


def local(adapter_gradients, sign_hash_keys, target_indices):
    resident_example, resident_rows = adapter_gradients.shape
    row_base = lax.axis_index("param") * jnp.int32(resident_rows)
    core = lax.axis_index("ec")
    swap = [(0, 1), (1, 0)]
    turn_count = 8
    rows_per_tile = resident_rows // turn_count
    scale_k = jnp.float32(K)
    param_count = lax.psum(1, "param")
    col_width = K // param_count
    half_width = col_width // 2

    hash_scalars = (sign_hash_keys[0] | 1, sign_hash_keys[1] | 1, sign_hash_keys[2], sign_hash_keys[3] | 1)
    hash_scalars, widened = lax.optimization_barrier((hash_scalars, adapter_gradients.astype(jnp.float32)))
    unit = (hash_scalars[3] & 1).astype(jnp.float32)
    partner = lax.ppermute(widened, "ec", swap) * unit
    partner = partner.astype(jnp.bfloat16)
    pair_gradients = jnp.where(
        core == 0,
        jnp.concatenate([adapter_gradients, partner], axis=0),
        jnp.concatenate([partner, adapter_gradients], axis=0),
    )
    owner = lax.iota(jnp.int32, param_count)[:, None] * col_width
    col_ids = (owner + core * half_width + lax.iota(jnp.int32, half_width)[None, :]).reshape(-1)
    row_terms, col_terms = hash_terms(hash_scalars, row_base, resident_rows, col_ids)
    totals = None
    for tile in range(turn_count):
        start_offset = tile * rows_per_tile
        gradient_slab = pair_gradients[:, start_offset:start_offset + rows_per_tile]
        signs = sign_block(hash_scalars, row_terms[start_offset:start_offset + rows_per_tile], col_terms)
        term = jnp.einsum(
            "cra,apj->pcrj",
            gradient_slab.reshape(2, resident_example, rows_per_tile),
            signs.reshape(rows_per_tile, param_count, half_width),
            preferred_element_type=jnp.float32,
        )
        totals = term if totals is None else totals + term

    blocks = totals.reshape(2 * param_count, resident_example, half_width)
    blocks = lax.all_to_all(blocks, ("param", "ec"), 0, 0, tiled=True)
    blocks = jnp.sum(blocks.reshape(param_count, 2, resident_example, half_width), axis=0)
    projected = jnp.transpose(blocks, (1, 0, 2)).reshape(resident_example, col_width)

    pool_rows = lax.all_gather(projected, ("ey", "ec"), axis=0, tiled=True)
    target_rows = jnp.take(pool_rows, target_indices, axis=0)
    partial_dots = jnp.dot(projected, target_rows.T, precision=lax.Precision.HIGHEST)
    own_squares = jnp.sum(projected * projected, axis=1)
    target_squares = jnp.sum(target_rows * target_rows, axis=1)
    packed = jnp.concatenate([partial_dots.reshape(-1), own_squares, target_squares])
    packed = butterfly_sum(packed, "param", param_count)
    dot_count = partial_dots.size
    dots = packed[:dot_count].reshape(partial_dots.shape)
    total_sq = packed[dot_count:dot_count + resident_example]
    target_sq = packed[dot_count + resident_example:]
    own_scale = jnp.sqrt(scale_k / (total_sq + norm_eps))
    target_scale = jnp.sqrt(scale_k / (target_sq + norm_eps))
    features = projected * own_scale[:, None]
    scores = dots * own_scale[:, None] * target_scale[None, :] / scale_k
    return (features, scores)


def solution(mesh):
    devices = mesh.devices
    pair_mesh = Mesh(devices.reshape(devices.shape[0], devices.shape[1] // 2, 2), ("param", "ey", "ec"))
    return jax.shard_map(
        local,
        mesh=pair_mesh,
        in_specs=(P(("ey", "ec"), "param"), P(), P()),
        out_specs=(P(("ey", "ec"), "param"), P(("ey", "ec"), None)),
        check_vma=False,
    )
```

```python
import jax
import jax.numpy as jnp
from jax import lax
from jax.sharding import Mesh, PartitionSpec as P

K = 8192


norm_eps = 1e-06


def hash_terms(sign_hash_keys, row_ids, col_ids):
    mult_row = sign_hash_keys[0] | 1
    mult_col = sign_hash_keys[1] | 1
    seed_add = sign_hash_keys[2]
    mix_mult = jnp.broadcast_to(sign_hash_keys[3] | 1, col_ids.shape)
    terms = jnp.stack([row_ids * mult_row + seed_add, col_ids * mult_col, mix_mult])
    terms = lax.optimization_barrier(terms)
    return terms[0], terms[1], terms[2]


def sign_block(mix_mult, row_terms, col_terms):
    hashed = row_terms[:, None] + col_terms[None, :]
    hashed = hashed ^ lax.shift_right_logical(hashed, jnp.full_like(hashed, 16))
    hashed = hashed * mix_mult[None, :]
    hashed = hashed ^ lax.shift_right_logical(hashed, jnp.full_like(hashed, 13))
    hashed = hashed * jnp.int32(-1028477387)
    hashed = hashed ^ lax.shift_right_logical(hashed, jnp.full_like(hashed, 16))
    return jnp.where(hashed < 0, jnp.bfloat16(1.0), jnp.bfloat16(-1.0))


def butterfly_sum(values, axis, count):
    distance = 1
    while distance < count:
        pairs = [(j, j ^ distance) for j in range(count)]
        values = values + lax.ppermute(values, axis, pairs)
        distance *= 2
    return values


def local(adapter_gradients, sign_hash_keys, target_indices):
    resident_example, resident_rows = adapter_gradients.shape
    row_base = lax.axis_index("param") * jnp.int32(resident_rows)
    core = lax.axis_index("ec")
    swap = [(0, 1), (1, 0)]
    turn_count = 8
    rows_per_tile = resident_rows // turn_count
    scale_k = jnp.float32(K)
    param_count = lax.psum(1, "param")
    col_width = K // param_count
    half_width = col_width // 2

    owner = lax.iota(jnp.int32, param_count)[:, None] * col_width
    col_ids = (owner + core * half_width + lax.iota(jnp.int32, half_width)[None, :]).reshape(-1)
    row_ids = row_base + lax.iota(jnp.int32, resident_rows)
    row_terms, col_terms, mix_mult = hash_terms(sign_hash_keys, row_ids, col_ids)
    unit = (mix_mult[:resident_rows] & 1).astype(jnp.float32)
    partner = lax.ppermute(adapter_gradients.astype(jnp.float32), "ec", swap) * unit[None, :]
    partner = partner.astype(jnp.bfloat16)
    pair_gradients = jnp.where(
        core == 0,
        jnp.concatenate([adapter_gradients, partner], axis=0),
        jnp.concatenate([partner, adapter_gradients], axis=0),
    )
    totals = None
    for tile in range(turn_count):
        start_offset = tile * rows_per_tile
        gradient_slab = pair_gradients[:, start_offset:start_offset + rows_per_tile]
        signs = sign_block(mix_mult, row_terms[start_offset:start_offset + rows_per_tile], col_terms)
        term = jnp.einsum(
            "cra,apj->pcrj",
            gradient_slab.reshape(2, resident_example, rows_per_tile),
            signs.reshape(rows_per_tile, param_count, half_width),
            preferred_element_type=jnp.float32,
        )
        totals = term if totals is None else totals + term

    blocks = totals.reshape(2 * param_count, resident_example, half_width)
    blocks = lax.all_to_all(blocks, ("param", "ec"), 0, 0, tiled=True)
    blocks = jnp.sum(blocks.reshape(param_count, 2, resident_example, half_width), axis=0)
    projected = jnp.transpose(blocks, (1, 0, 2)).reshape(resident_example, col_width)

    pool_rows = lax.all_gather(projected, ("ey", "ec"), axis=0, tiled=True)
    target_rows = jnp.take(pool_rows, target_indices, axis=0)
    partial_dots = jnp.dot(projected, target_rows.T, precision=lax.Precision.HIGHEST)
    own_squares = jnp.sum(projected * projected, axis=1)
    target_squares = jnp.sum(target_rows * target_rows, axis=1)
    packed = jnp.concatenate([partial_dots.reshape(-1), own_squares, target_squares])
    packed = butterfly_sum(packed, "param", param_count)
    dot_count = partial_dots.size
    dots = packed[:dot_count].reshape(partial_dots.shape)
    total_sq = packed[dot_count:dot_count + resident_example]
    target_sq = packed[dot_count + resident_example:]
    own_scale = jnp.sqrt(scale_k / (total_sq + norm_eps))
    target_scale = jnp.sqrt(scale_k / (target_sq + norm_eps))
    features = projected * own_scale[:, None]
    scores = dots * own_scale[:, None] * target_scale[None, :] / scale_k
    return (features, scores)


def solution(mesh):
    devices = mesh.devices
    pair_mesh = Mesh(devices.reshape(devices.shape[0], devices.shape[1] // 2, 2), ("param", "ey", "ec"))
    return jax.shard_map(
        local,
        mesh=pair_mesh,
        in_specs=(P(("ey", "ec"), "param"), P(), P()),
        out_specs=(P(("ey", "ec"), "param"), P(("ey", "ec"), None)),
        check_vma=False,
    )
```

```python
import jax
import jax.numpy as jnp
from jax import lax
from jax.sharding import Mesh, PartitionSpec as P

K = 8192


norm_eps = 1e-06


def hash_terms(sign_hash_keys, first_row, row_count, col_ids):
    mult_row = sign_hash_keys[0] | 1
    mult_col = sign_hash_keys[1] | 1
    seed_add = sign_hash_keys[2]
    row_ids = first_row + lax.iota(jnp.int32, row_count)
    return row_ids * mult_row + seed_add, col_ids * mult_col


def sign_block(sign_hash_keys, row_terms, col_terms):
    mix_mult = sign_hash_keys[3] | 1
    hashed = row_terms[:, None] + col_terms[None, :]
    hashed = hashed ^ lax.shift_right_logical(hashed, jnp.full_like(hashed, 16))
    hashed = hashed * mix_mult
    hashed = hashed ^ lax.shift_right_logical(hashed, jnp.full_like(hashed, 13))
    hashed = hashed * jnp.int32(-1028477387)
    hashed = hashed ^ lax.shift_right_logical(hashed, jnp.full_like(hashed, 16))
    return jnp.where(hashed < 0, jnp.bfloat16(1.0), jnp.bfloat16(-1.0))


def butterfly_sum(values, axis, count):
    distance = 1
    while distance < count:
        pairs = [(j, j ^ distance) for j in range(count)]
        values = values + lax.ppermute(values, axis, pairs)
        distance *= 2
    return values


def local(adapter_gradients, sign_hash_keys, target_indices):
    resident_example, resident_rows = adapter_gradients.shape
    row_base = lax.axis_index("param") * jnp.int32(resident_rows)
    core = lax.axis_index("ec")
    swap = [(0, 1), (1, 0)]
    turn_count = 8
    rows_per_tile = resident_rows // turn_count
    scale_k = jnp.float32(K)
    param_count = lax.psum(1, "param")
    col_width = K // param_count
    half_width = col_width // 2

    unit = ((sign_hash_keys[3] | 1) & 1).astype(jnp.float32)
    partner = lax.ppermute(adapter_gradients.astype(jnp.float32), "ec", swap) * unit
    partner = partner.astype(jnp.bfloat16)
    pair_gradients = jnp.where(
        core == 0,
        jnp.concatenate([adapter_gradients, partner], axis=0),
        jnp.concatenate([partner, adapter_gradients], axis=0),
    )
    owner = lax.iota(jnp.int32, param_count)[:, None] * col_width
    col_ids = (owner + core * half_width + lax.iota(jnp.int32, half_width)[None, :]).reshape(-1)
    row_terms, col_terms = hash_terms(sign_hash_keys, row_base, resident_rows, col_ids)
    totals = None
    for tile in range(turn_count):
        start_offset = tile * rows_per_tile
        gradient_slab = pair_gradients[:, start_offset:start_offset + rows_per_tile]
        signs = sign_block(sign_hash_keys, row_terms[start_offset:start_offset + rows_per_tile], col_terms)
        term = jnp.einsum(
            "cra,apj->pcrj",
            gradient_slab.reshape(2, resident_example, rows_per_tile),
            signs.reshape(rows_per_tile, param_count, half_width),
            preferred_element_type=jnp.float32,
        )
        totals = term if totals is None else totals + term

    blocks = totals.reshape(2 * param_count, resident_example, half_width)
    blocks = lax.all_to_all(blocks, ("param", "ec"), 0, 0, tiled=True)
    blocks = jnp.sum(blocks.reshape(param_count, 2, resident_example, half_width), axis=0)
    projected = jnp.transpose(blocks, (1, 0, 2)).reshape(resident_example, col_width)

    pool_rows = lax.all_gather(projected, ("ey", "ec"), axis=0, tiled=True)
    picks = (target_indices[:, None] == lax.iota(jnp.int32, pool_rows.shape[0])[None, :]).astype(jnp.float32)
    target_rows = jnp.dot(picks, pool_rows, precision=lax.Precision.HIGHEST)
    partial_dots = jnp.dot(projected, target_rows.T, precision=lax.Precision.HIGHEST)
    own_squares = jnp.sum(projected * projected, axis=1)
    target_squares = jnp.sum(target_rows * target_rows, axis=1)
    packed = jnp.concatenate([partial_dots.reshape(-1), own_squares, target_squares])
    packed = butterfly_sum(packed, "param", param_count)
    dot_count = partial_dots.size
    dots = packed[:dot_count].reshape(partial_dots.shape)
    total_sq = packed[dot_count:dot_count + resident_example]
    target_sq = packed[dot_count + resident_example:]
    own_scale = jnp.sqrt(scale_k / (total_sq + norm_eps))
    target_scale = jnp.sqrt(scale_k / (target_sq + norm_eps))
    features = projected * own_scale[:, None]
    scores = dots * own_scale[:, None] * target_scale[None, :] / scale_k
    return (features, scores)


def solution(mesh):
    devices = mesh.devices
    pair_mesh = Mesh(devices.reshape(devices.shape[0], devices.shape[1] // 2, 2), ("param", "ey", "ec"))
    return jax.shard_map(
        local,
        mesh=pair_mesh,
        in_specs=(P(("ey", "ec"), "param"), P(), P()),
        out_specs=(P(("ey", "ec"), "param"), P(("ey", "ec"), None)),
        check_vma=False,
    )
```

```python
import jax
import jax.numpy as jnp
from jax import lax
from jax.sharding import Mesh, PartitionSpec as P

K = 8192


norm_eps = 1e-06


def hash_terms(sign_hash_keys, first_row, row_count, col_ids):
    mult_row = sign_hash_keys[0] | 1
    mult_col = sign_hash_keys[1] | 1
    seed_add = sign_hash_keys[2]
    row_ids = first_row + lax.iota(jnp.int32, row_count)
    return row_ids * mult_row + seed_add, col_ids * mult_col


def sign_block(sign_hash_keys, row_terms, col_terms):
    mix_mult = sign_hash_keys[3] | 1
    hashed = row_terms[:, None] + col_terms[None, :]
    hashed = hashed ^ lax.shift_right_logical(hashed, jnp.full_like(hashed, 16))
    hashed = hashed * mix_mult
    hashed = hashed ^ lax.shift_right_logical(hashed, jnp.full_like(hashed, 13))
    hashed = hashed * jnp.int32(-1028477387)
    hashed = hashed ^ lax.shift_right_logical(hashed, jnp.full_like(hashed, 16))
    return jnp.where(hashed < 0, jnp.bfloat16(1.0), jnp.bfloat16(-1.0))


def butterfly_sum(values, axis, count):
    distance = 1
    while distance < count:
        pairs = [(j, j ^ distance) for j in range(count)]
        values = values + lax.ppermute(values, axis, pairs)
        distance *= 2
    return values


def local(adapter_gradients, sign_hash_keys, target_indices):
    resident_example, resident_rows = adapter_gradients.shape
    row_base = lax.axis_index("param") * jnp.int32(resident_rows)
    core = lax.axis_index("ec")
    swap = [(0, 1), (1, 0)]
    turn_count = 4
    rows_per_tile = resident_rows // turn_count
    scale_k = jnp.float32(K)
    param_count = lax.psum(1, "param")
    col_width = K // param_count
    half_width = col_width // 2

    unit = ((sign_hash_keys[3] | 1) & 1).astype(jnp.float32)
    partner = lax.ppermute(adapter_gradients.astype(jnp.float32), "ec", swap) * unit
    partner = partner.astype(jnp.bfloat16)
    pair_gradients = jnp.where(
        core == 0,
        jnp.concatenate([adapter_gradients, partner], axis=0),
        jnp.concatenate([partner, adapter_gradients], axis=0),
    )
    owner = lax.iota(jnp.int32, param_count)[:, None] * col_width
    col_ids = (owner + core * half_width + lax.iota(jnp.int32, half_width)[None, :]).reshape(-1)
    row_terms, col_terms = hash_terms(sign_hash_keys, row_base, resident_rows, col_ids)
    totals = None
    for tile in range(turn_count):
        start_offset = tile * rows_per_tile
        gradient_slab = pair_gradients[:, start_offset:start_offset + rows_per_tile]
        signs = sign_block(sign_hash_keys, row_terms[start_offset:start_offset + rows_per_tile], col_terms)
        term = jnp.einsum(
            "cra,apj->pcrj",
            gradient_slab.reshape(2, resident_example, rows_per_tile),
            signs.reshape(rows_per_tile, param_count, half_width),
            preferred_element_type=jnp.float32,
        )
        totals = term if totals is None else totals + term

    blocks = totals.reshape(2 * param_count, resident_example, half_width)
    blocks = lax.all_to_all(blocks, ("param", "ec"), 0, 0, tiled=True)
    blocks = jnp.sum(blocks.reshape(param_count, 2, resident_example, half_width), axis=0)
    projected = jnp.transpose(blocks, (1, 0, 2)).reshape(resident_example, col_width)

    pool_rows = lax.all_gather(projected, ("ey", "ec"), axis=0, tiled=True)
    picks = (target_indices[:, None] == lax.iota(jnp.int32, pool_rows.shape[0])[None, :]).astype(jnp.float32)
    target_rows = jnp.dot(picks, pool_rows, precision=lax.Precision.HIGHEST)
    partial_dots = jnp.dot(projected, target_rows.T, precision=lax.Precision.HIGHEST)
    own_squares = jnp.sum(projected * projected, axis=1)
    target_squares = jnp.sum(target_rows * target_rows, axis=1)
    packed = jnp.concatenate([partial_dots.reshape(-1), own_squares, target_squares])
    packed = butterfly_sum(packed, "param", param_count)
    dot_count = partial_dots.size
    dots = packed[:dot_count].reshape(partial_dots.shape)
    total_sq = packed[dot_count:dot_count + resident_example]
    target_sq = packed[dot_count + resident_example:]
    own_scale = jnp.sqrt(scale_k / (total_sq + norm_eps))
    target_scale = jnp.sqrt(scale_k / (target_sq + norm_eps))
    features = projected * own_scale[:, None]
    scores = dots * own_scale[:, None] * target_scale[None, :] / scale_k
    return (features, scores)


def solution(mesh):
    devices = mesh.devices
    pair_mesh = Mesh(devices.reshape(devices.shape[0], devices.shape[1] // 2, 2), ("param", "ey", "ec"))
    return jax.shard_map(
        local,
        mesh=pair_mesh,
        in_specs=(P(("ey", "ec"), "param"), P(), P()),
        out_specs=(P(("ey", "ec"), "param"), P(("ey", "ec"), None)),
        check_vma=False,
    )
```

```python
import jax
import jax.numpy as jnp
from jax import lax
from jax.sharding import Mesh, PartitionSpec as P

K = 8192


norm_eps = 1e-06


def hash_terms(sign_hash_keys, first_row, row_count, col_ids):
    mult_row = sign_hash_keys[0] | 1
    mult_col = sign_hash_keys[1] | 1
    seed_add = sign_hash_keys[2]
    row_ids = first_row + lax.iota(jnp.int32, row_count)
    return row_ids * mult_row + seed_add, col_ids * mult_col


def sign_block(sign_hash_keys, row_terms, col_terms):
    mix_mult = sign_hash_keys[3] | 1
    hashed = row_terms[:, None] + col_terms[None, :]
    hashed = hashed ^ lax.shift_right_logical(hashed, jnp.full_like(hashed, 16))
    hashed = hashed * mix_mult
    hashed = hashed ^ lax.shift_right_logical(hashed, jnp.full_like(hashed, 13))
    hashed = hashed * jnp.int32(-1028477387)
    hashed = hashed ^ lax.shift_right_logical(hashed, jnp.full_like(hashed, 16))
    return jnp.where(hashed < 0, jnp.bfloat16(1.0), jnp.bfloat16(-1.0))


def butterfly_sum(values, axis, count):
    distance = 1
    while distance < count:
        pairs = [(j, j ^ distance) for j in range(count)]
        values = values + lax.ppermute(values, axis, pairs)
        distance *= 2
    return values


def local(adapter_gradients, sign_hash_keys, target_indices):
    resident_example, resident_rows = adapter_gradients.shape
    row_base = lax.axis_index("param") * jnp.int32(resident_rows)
    core = lax.axis_index("ec")
    swap = [(0, 1), (1, 0)]
    turn_count = 2
    rows_per_tile = resident_rows // turn_count
    scale_k = jnp.float32(K)
    param_count = lax.psum(1, "param")
    col_width = K // param_count
    half_width = col_width // 2

    unit = ((sign_hash_keys[3] | 1) & 1).astype(jnp.float32)
    partner = lax.ppermute(adapter_gradients.astype(jnp.float32), "ec", swap) * unit
    partner = partner.astype(jnp.bfloat16)
    pair_gradients = jnp.where(
        core == 0,
        jnp.concatenate([adapter_gradients, partner], axis=0),
        jnp.concatenate([partner, adapter_gradients], axis=0),
    )
    owner = lax.iota(jnp.int32, param_count)[:, None] * col_width
    col_ids = (owner + core * half_width + lax.iota(jnp.int32, half_width)[None, :]).reshape(-1)
    row_terms, col_terms = hash_terms(sign_hash_keys, row_base, resident_rows, col_ids)
    totals = None
    for tile in range(turn_count):
        start_offset = tile * rows_per_tile
        gradient_slab = pair_gradients[:, start_offset:start_offset + rows_per_tile]
        signs = sign_block(sign_hash_keys, row_terms[start_offset:start_offset + rows_per_tile], col_terms)
        term = jnp.einsum(
            "cra,apj->pcrj",
            gradient_slab.reshape(2, resident_example, rows_per_tile),
            signs.reshape(rows_per_tile, param_count, half_width),
            preferred_element_type=jnp.float32,
        )
        totals = term if totals is None else totals + term

    blocks = totals.reshape(2 * param_count, resident_example, half_width)
    blocks = lax.all_to_all(blocks, ("param", "ec"), 0, 0, tiled=True)
    blocks = jnp.sum(blocks.reshape(param_count, 2, resident_example, half_width), axis=0)
    projected = jnp.transpose(blocks, (1, 0, 2)).reshape(resident_example, col_width)

    pool_rows = lax.all_gather(projected, ("ey", "ec"), axis=0, tiled=True)
    picks = (target_indices[:, None] == lax.iota(jnp.int32, pool_rows.shape[0])[None, :]).astype(jnp.float32)
    target_rows = jnp.dot(picks, pool_rows, precision=lax.Precision.HIGHEST)
    partial_dots = jnp.dot(projected, target_rows.T, precision=lax.Precision.HIGHEST)
    own_squares = jnp.sum(projected * projected, axis=1)
    target_squares = jnp.sum(target_rows * target_rows, axis=1)
    packed = jnp.concatenate([partial_dots.reshape(-1), own_squares, target_squares])
    packed = butterfly_sum(packed, "param", param_count)
    dot_count = partial_dots.size
    dots = packed[:dot_count].reshape(partial_dots.shape)
    total_sq = packed[dot_count:dot_count + resident_example]
    target_sq = packed[dot_count + resident_example:]
    own_scale = jnp.sqrt(scale_k / (total_sq + norm_eps))
    target_scale = jnp.sqrt(scale_k / (target_sq + norm_eps))
    features = projected * own_scale[:, None]
    scores = dots * own_scale[:, None] * target_scale[None, :] / scale_k
    return (features, scores)


def solution(mesh):
    devices = mesh.devices
    pair_mesh = Mesh(devices.reshape(devices.shape[0], devices.shape[1] // 2, 2), ("param", "ey", "ec"))
    return jax.shard_map(
        local,
        mesh=pair_mesh,
        in_specs=(P(("ey", "ec"), "param"), P(), P()),
        out_specs=(P(("ey", "ec"), "param"), P(("ey", "ec"), None)),
        check_vma=False,
    )
```

```python
import jax
import jax.numpy as jnp
from jax import lax
from jax.sharding import Mesh, PartitionSpec as P

K = 8192


norm_eps = 1e-06


def hash_terms(sign_hash_keys, first_row, row_count, col_ids):
    mult_row = sign_hash_keys[0] | 1
    mult_col = sign_hash_keys[1] | 1
    seed_add = sign_hash_keys[2]
    row_ids = first_row + lax.iota(jnp.int32, row_count)
    return row_ids * mult_row + seed_add, col_ids * mult_col


def sign_block(sign_hash_keys, row_terms, col_terms):
    mix_mult = sign_hash_keys[3] | 1
    hashed = row_terms[:, None] + col_terms[None, :]
    hashed = hashed ^ lax.shift_right_logical(hashed, jnp.full_like(hashed, 16))
    hashed = hashed * mix_mult
    hashed = hashed ^ lax.shift_right_logical(hashed, jnp.full_like(hashed, 13))
    hashed = hashed * jnp.int32(-1028477387)
    hashed = hashed ^ lax.shift_right_logical(hashed, jnp.full_like(hashed, 16))
    return jnp.where(hashed < 0, jnp.bfloat16(1.0), jnp.bfloat16(-1.0))


def butterfly_sum(values, axis, count):
    distance = 1
    while distance < count:
        pairs = [(j, j ^ distance) for j in range(count)]
        values = values + lax.ppermute(values, axis, pairs)
        distance *= 2
    return values


def local(adapter_gradients, sign_hash_keys, target_indices):
    resident_example, resident_rows = adapter_gradients.shape
    row_base = lax.axis_index("param") * jnp.int32(resident_rows)
    core = lax.axis_index("ec")
    swap = [(0, 1), (1, 0)]
    turn_count = 2
    rows_per_tile = resident_rows // turn_count
    scale_k = jnp.float32(K)
    param_count = lax.psum(1, "param")
    col_width = K // param_count
    half_width = col_width // 2

    unit = ((sign_hash_keys[3] | 1) & 1).astype(jnp.float32)
    partner = lax.ppermute(adapter_gradients.astype(jnp.float32), "ec", swap) * unit
    partner = partner.astype(jnp.bfloat16)
    pair_gradients = jnp.where(
        core == 0,
        jnp.concatenate([adapter_gradients, partner], axis=0),
        jnp.concatenate([partner, adapter_gradients], axis=0),
    )
    owner = lax.iota(jnp.int32, param_count)[:, None] * col_width
    col_ids = (owner + core * half_width + lax.iota(jnp.int32, half_width)[None, :]).reshape(-1)
    row_terms, col_terms = hash_terms(sign_hash_keys, row_base, resident_rows, col_ids)
    totals = None
    for tile in range(turn_count):
        start_offset = tile * rows_per_tile
        gradient_slab = pair_gradients[:, start_offset:start_offset + rows_per_tile]
        signs = sign_block(sign_hash_keys, row_terms[start_offset:start_offset + rows_per_tile], col_terms)
        term = jnp.einsum(
            "cra,apj->pcrj",
            gradient_slab.reshape(2, resident_example, rows_per_tile),
            signs.reshape(rows_per_tile, param_count, half_width),
            preferred_element_type=jnp.float32,
        )
        totals = term if totals is None else totals + term

    blocks = totals.reshape(2 * param_count, resident_example, half_width)
    blocks = lax.all_to_all(blocks, ("param", "ec"), 0, 0, tiled=True)
    blocks = jnp.sum(blocks.reshape(param_count, 2, resident_example, half_width), axis=0)
    projected = jnp.transpose(blocks, (1, 0, 2)).reshape(resident_example, col_width)

    pool_rows = lax.all_gather(projected, ("ey", "ec"), axis=0, tiled=True)
    picks = (target_indices[:, None] == lax.iota(jnp.int32, pool_rows.shape[0])[None, :]).astype(jnp.float32)
    target_rows = jnp.dot(picks, pool_rows, precision=lax.Precision.HIGHEST)
    partial_dots = jnp.dot(projected, target_rows.T, precision=lax.Precision.HIGHEST)
    own_squares = jnp.sum(projected * projected, axis=1)
    target_squares = jnp.sum(target_rows * target_rows, axis=1)
    packed = jnp.concatenate([partial_dots.reshape(-1), own_squares, target_squares])
    packed = butterfly_sum(packed, "param", param_count)
    dot_count = partial_dots.size
    dots = packed[:dot_count].reshape(partial_dots.shape)
    total_sq = packed[dot_count:dot_count + resident_example]
    target_sq = packed[dot_count + resident_example:]
    own_scale = jnp.sqrt(scale_k / (total_sq + norm_eps))
    target_scale = jnp.sqrt(scale_k / (target_sq + norm_eps))
    features = projected * own_scale[:, None]
    scores = dots * own_scale[:, None] * (target_scale / scale_k)[None, :]
    return (features, scores)


def solution(mesh):
    devices = mesh.devices
    pair_mesh = Mesh(devices.reshape(devices.shape[0], devices.shape[1] // 2, 2), ("param", "ey", "ec"))
    return jax.shard_map(
        local,
        mesh=pair_mesh,
        in_specs=(P(("ey", "ec"), "param"), P(), P()),
        out_specs=(P(("ey", "ec"), "param"), P(("ey", "ec"), None)),
        check_vma=False,
    )
```
